512 devices in a mesh: dp: 4 (over x), ctx: 4 (over y_lo), tp: 32 (over z, y_hi, core).
Axes of the slice: x: 4, y: 8 (y_hi: 2, y_lo: 4; y = y_hi * 4 + y_lo), z: 8, core: 2. Of those that a mesh axis runs over, the one named last changes fastest.
Arguments:
- cotangent: bfloat16 [6144, 4096], P(('dp', 'ctx')), may hold values from -6 to 6
- gate_pre: bfloat16 [6144, 16384], P(('dp', 'ctx'), 'tp'), may hold values from -6 to 6
- up_pre: bfloat16 [6144, 16384], P(('dp', 'ctx'), 'tp'), may hold values from -6 to 6
- w_down: bfloat16 [4096, 16384], P(('dp', 'ctx'), 'tp'), may hold values from -0.046875 to 0.046875
Outputs:
- grad_gate: bfloat16 [6144, 16384], P(('dp', 'ctx'), 'tp')
- grad_up: bfloat16 [6144, 16384], P(('dp', 'ctx'), 'tp')
- grad_down: bfloat16 [4096, 16384], P(('dp', 'ctx'), 'tp')
The draws below stay inside these ranges and needn't reach their ends.
All inputs are finite; a program needn't handle non-finite values.
Results may differ from the reference program's by a relative error of at most 0.018.
Values may be sent and summed in bfloat16 or wider, within the bound.
No kernel may reach another device: no remote copies, remote signals or barrier semaphores. Data moves between devices by JAX's collectives and lax.ppermute only.
A program may use at most 64 MiB of HBM per device.

```python
import jax
import jax.numpy as jnp
from jax import lax

D = 4096
FF = 16384
ROWS = 384
GROUPS = 16
TOKENS = 6144


def raised(values, rng, source, target, blocks, factor):
    owner, partner = [(jnp.arange(values.shape[axis_at]) // (values.shape[axis_at] // blocks)).reshape([-1 if axis == axis_at else 1 for axis in range(values.ndim)]) for axis_at in (source, target)]
    chosen = jax.random.permutation(rng, blocks)[partner]
    strong = (owner == chosen) | (owner == (partner + blocks // 2) % blocks)
    return jnp.where(strong, factor * values, values)


def steps_of(key, dims, shards, low, high):
    def one(dim, shards_of):
        steps = jax.random.uniform(jax.random.fold_in(jax.random.fold_in(key, 6), dim), (shards_of,), jnp.float32, low / len(shards), high / len(shards))
        return jnp.repeat(jnp.exp(steps), dims[dim] // shards_of).reshape((-1,) + (1,) * (len(dims) - dim - 1))

    factor_of = one(*shards[0])
    for cut in shards[1:]:
        factor_of = factor_of * one(*cut)
    return factor_of


def noise(key, shape, width, limit, shards=(), kind=jnp.bfloat16):
    loudness = steps_of(key, shape, shards, -0.22, 0.18) if shards else 1.0
    result = jax.random.normal(key, shape, jnp.float32) * width * loudness
    return jnp.minimum(jnp.maximum(result, -limit), limit).astype(kind)


def gaussian_with(rng, extent, width, bound, cuts, heavy, kind=jnp.bfloat16):
    result = width * jax.random.normal(rng, extent, jnp.float32)
    if cuts:
        result = result * steps_of(rng, extent, cuts, -0.22, 0.18)
    return jnp.clip(raised(result, jax.random.fold_in(rng, 3), *heavy), -bound, bound).astype(kind)


def setup_inputs(seed: int = 0) -> dict:
    keys = jax.random.split(jax.random.key(seed), 5)
    cotangent = gaussian_with(keys[0], (TOKENS, D), 1.0, 6.0, ((0, 16),), (0, 1, 16, 2.0))
    gate_pre = noise(keys[1], (TOKENS, FF), 1.0, 6.0, ((0, 16), (1, 32)))
    up_pre = noise(keys[2], (TOKENS, FF), 1.0, 6.0, ((0, 16), (1, 32)))
    w_down = noise(keys[3], (D, FF), FF ** -0.5, 0.046875, ((0, 16), (1, 32)))
    return dict(cotangent=cotangent, gate_pre=gate_pre, up_pre=up_pre, w_down=w_down)


def reference(cotangent, gate_pre, up_pre, w_down):
    gate_wide = gate_pre.astype(jnp.float32)
    up_wide = up_pre.astype(jnp.float32)
    sigmoid_gate = 1.0 / (1.0 + jnp.exp(-gate_wide))
    activated = gate_wide * sigmoid_gate
    hidden = (activated * up_wide).astype(jnp.bfloat16)
    grad_hidden = jnp.dot(cotangent, w_down, preferred_element_type=jnp.float32)
    grad_gate = (grad_hidden * up_wide * sigmoid_gate * (1.0 + gate_wide * (1.0 - sigmoid_gate))).astype(jnp.bfloat16)
    grad_up = (grad_hidden * activated).astype(jnp.bfloat16)
    cot_groups = cotangent.reshape(GROUPS, ROWS, D)
    hid_groups = hidden.reshape(GROUPS, ROWS, FF)

    def accumulate(running, pair):
        cot_block, hid_block = pair
        partial_value = jnp.dot(cot_block.T, hid_block, preferred_element_type=jnp.float32).astype(jnp.bfloat16)
        return running + partial_value.astype(jnp.float32), None

    summed, _ = lax.scan(accumulate, jnp.zeros((D, FF), jnp.float32), (cot_groups, hid_groups))
    grad_down = (summed / GROUPS).astype(jnp.bfloat16)
    return grad_gate, grad_up, grad_down
```

```python
import jax
import jax.numpy as jnp
from jax import lax
from jax.sharding import PartitionSpec as P


def _line(x, axis, n, k):
    return lax.ppermute(x, axis, [(i, i + k) for i in range(n) if 0 <= i + k < n])


def _ring(x, axis, n, k):
    return lax.ppermute(x, axis, [(i, (i + k) % n) for i in range(n)])


def gather_line(x, axis, n):
    c = lax.axis_index(axis)
    parts = [_line(x, axis, n, n - 1 - j) if j < n - 1 else x for j in range(n)]
    parts += [_line(x, axis, n, -k) for k in range(1, n)]
    stack = jnp.stack(parts)
    out = lax.dynamic_slice_in_dim(stack, n - 1 - c, n, axis=0)
    return out.reshape((n * x.shape[0],) + x.shape[1:])


def gather_ring4(x, axis):
    h = x.shape[0] // 2
    p1 = _ring(x, axis, 4, 1)
    m1 = _ring(x, axis, 4, -1)
    f = _ring(p1[:h], axis, 4, 1)
    g = _ring(m1[h:], axis, 4, -1)
    return [x, m1, jnp.concatenate([f, g]), p1]


def scatter_ring4(blocks, axis):
    b0, b1, b2, b3 = blocks
    h = b0.shape[0] // 2
    bf = jnp.bfloat16
    s1p = _ring(b1[h:].astype(bf), axis, 4, 1)
    x1 = _ring(b2[:h].astype(bf), axis, 4, 1)
    s1m = _ring(b3[:h].astype(bf), axis, 4, -1)
    y1 = _ring(b2[h:].astype(bf), axis, 4, -1)
    s2p = _ring((b1[:h] + x1.astype(jnp.float32)).astype(bf), axis, 4, 1)
    s2m = _ring((b3[h:] + y1.astype(jnp.float32)).astype(bf), axis, 4, -1)
    f32 = jnp.float32
    top = b0[:h] + s2p.astype(f32) + s1m.astype(f32)
    bot = b0[h:] + s1p.astype(f32) + s2m.astype(f32)
    return jnp.concatenate([top, bot])


def scatter_line(x, axis, n):
    c = lax.axis_index(axis)
    rows = x.shape[0] // n
    acc = lax.dynamic_slice_in_dim(x, c * rows, rows, axis=0)
    for k in list(range(1, n)) + list(range(-n + 1, 0)):
        part = lax.dynamic_slice_in_dim(x, jnp.clip(c + k, 0, n - 1) * rows, rows, axis=0)
        acc = acc + _line(part.astype(jnp.bfloat16), axis, n, k).astype(jnp.float32)
    return acc


def local(cotangent, gate_pre, up_pre, w_down):
    gate_wide = gate_pre.astype(jnp.float32)
    up_wide = up_pre.astype(jnp.float32)
    sigmoid_gate = jax.nn.sigmoid(gate_wide)
    activated = gate_wide * sigmoid_gate
    hidden = (activated * up_wide).astype(jnp.bfloat16)
    ndp = lax.axis_size("dp")
    nctx = lax.axis_size("ctx")
    groups = ndp * nctx
    a = lax.axis_index("dp")

    w_ctx = gather_line(w_down, "ctx", nctx)
    span = w_ctx.shape[0]
    grad_hidden = None
    for k, blk in enumerate(gather_ring4(w_ctx, "dp")):
        cols = lax.dynamic_slice_in_dim(cotangent, ((a + k) % ndp) * span, span, axis=1)
        term = jnp.dot(cols, blk, preferred_element_type=jnp.float32)
        grad_hidden = term if grad_hidden is None else grad_hidden + term
    grad_gate = (
        grad_hidden * up_wide * sigmoid_gate * (1.0 + gate_wide * (1.0 - sigmoid_gate))
    ).astype(jnp.bfloat16)
    grad_up = (grad_hidden * activated).astype(jnp.bfloat16)

    partial = lax.dot_general(
        cotangent, hidden, (((0,), (0,)), ((), ())), preferred_element_type=jnp.float32
    )
    blocks = [lax.dynamic_slice_in_dim(partial, ((a + k) % ndp) * span, span, axis=0) for k in range(4)]
    reduced = scatter_ring4(blocks, "dp")
    summed = scatter_line(reduced, "ctx", nctx)
    grad_down = (summed / groups).astype(jnp.bfloat16)
    return (grad_gate, grad_up, grad_down)


def solution(mesh):
    in_specs = (
        P(("dp", "ctx"), None),
        P(("dp", "ctx"), "tp"),
        P(("dp", "ctx"), "tp"),
        P(("dp", "ctx"), "tp"),
    )
    out_specs = (P(("dp", "ctx"), "tp"), P(("dp", "ctx"), "tp"), P(("dp", "ctx"), "tp"))
    return jax.shard_map(local, mesh=mesh, in_specs=in_specs, out_specs=out_specs, check_vma=False)
```

```python
import jax
import jax.numpy as jnp
from jax import lax
from jax.sharding import PartitionSpec as P


def _line(x, axis, n, k):
    return lax.ppermute(x, axis, [(i, i + k) for i in range(n) if 0 <= i + k < n])


def _ring(x, axis, n, k):
    return lax.ppermute(x, axis, [(i, (i + k) % n) for i in range(n)])


def gather_line(x, axis, n):
    c = lax.axis_index(axis)
    parts = [x] + [_ring(x, axis, n, k) for k in range(1, n)]
    stack = jnp.stack(parts[::-1] + parts[:0:-1])
    out = lax.dynamic_slice_in_dim(stack, n - 1 - c, n, axis=0)
    return out.reshape((n * x.shape[0],) + x.shape[1:])


def gather_ring4(x, axis):
    h = x.shape[0] // 2
    p1 = _ring(x, axis, 4, 1)
    m1 = _ring(x, axis, 4, -1)
    f = _ring(p1[:h], axis, 4, 1)
    g = _ring(m1[h:], axis, 4, -1)
    return [x, m1, jnp.concatenate([f, g]), p1]


def scatter_ring4(blocks, axis):
    b0, b1, b2, b3 = blocks
    h = b0.shape[0] // 2
    bf = jnp.bfloat16
    got_p = _ring(jnp.concatenate([b1[h:], b2[:h]]).astype(bf), axis, 4, 1)
    got_m = _ring(jnp.concatenate([b3[:h], b2[h:]]).astype(bf), axis, 4, -1)
    s1p, x1 = got_p[:h], got_p[h:]
    s1m, y1 = got_m[:h], got_m[h:]
    s2p = _ring((b1[:h] + x1.astype(jnp.float32)).astype(bf), axis, 4, 1)
    s2m = _ring((b3[h:] + y1.astype(jnp.float32)).astype(bf), axis, 4, -1)
    f32 = jnp.float32
    top = b0[:h] + s2p.astype(f32) + s1m.astype(f32)
    bot = b0[h:] + s1p.astype(f32) + s2m.astype(f32)
    return jnp.concatenate([top, bot])


def scatter_line(x, axis, n):
    c = lax.axis_index(axis)
    rows = x.shape[0] // n
    acc = lax.dynamic_slice_in_dim(x, c * rows, rows, axis=0)
    for k in range(1, n):
        part = lax.dynamic_slice_in_dim(x, ((c + k) % n) * rows, rows, axis=0)
        acc = acc + _ring(part.astype(jnp.bfloat16), axis, n, k).astype(jnp.float32)
    return acc


def local(cotangent, gate_pre, up_pre, w_down):
    gate_wide = gate_pre.astype(jnp.float32)
    up_wide = up_pre.astype(jnp.float32)
    sigmoid_gate = jax.nn.sigmoid(gate_wide)
    activated = gate_wide * sigmoid_gate
    hidden = (activated * up_wide).astype(jnp.bfloat16)
    ndp = lax.axis_size("dp")
    nctx = lax.axis_size("ctx")
    groups = ndp * nctx
    a = lax.axis_index("dp")

    w_ctx = gather_line(w_down, "ctx", nctx)
    span = w_ctx.shape[0]
    grad_hidden = None
    for k, blk in enumerate(gather_ring4(w_ctx, "dp")):
        cols = lax.dynamic_slice_in_dim(cotangent, ((a + k) % ndp) * span, span, axis=1)
        term = jnp.dot(cols, blk, preferred_element_type=jnp.float32)
        grad_hidden = term if grad_hidden is None else grad_hidden + term
    grad_gate = (
        grad_hidden * up_wide * sigmoid_gate * (1.0 + gate_wide * (1.0 - sigmoid_gate))
    ).astype(jnp.bfloat16)
    grad_up = (grad_hidden * activated).astype(jnp.bfloat16)

    partial = lax.dot_general(
        cotangent, hidden, (((0,), (0,)), ((), ())), preferred_element_type=jnp.float32
    )
    blocks = [lax.dynamic_slice_in_dim(partial, ((a + k) % ndp) * span, span, axis=0) for k in range(4)]
    reduced = scatter_ring4(blocks, "dp")
    summed = scatter_line(reduced, "ctx", nctx)
    grad_down = (summed / groups).astype(jnp.bfloat16)
    return (grad_gate, grad_up, grad_down)


def solution(mesh):
    in_specs = (
        P(("dp", "ctx"), None),
        P(("dp", "ctx"), "tp"),
        P(("dp", "ctx"), "tp"),
        P(("dp", "ctx"), "tp"),
    )
    out_specs = (P(("dp", "ctx"), "tp"), P(("dp", "ctx"), "tp"), P(("dp", "ctx"), "tp"))
    return jax.shard_map(local, mesh=mesh, in_specs=in_specs, out_specs=out_specs, check_vma=False)
```

```python
import jax
import jax.numpy as jnp
from jax import lax
from jax.sharding import PartitionSpec as P


def _line(x, axis, n, k):
    return lax.ppermute(x, axis, [(i, i + k) for i in range(n) if 0 <= i + k < n])


def _ring(x, axis, n, k):
    return lax.ppermute(x, axis, [(i, (i + k) % n) for i in range(n)])


def gather_line(x, axis, n):
    c = lax.axis_index(axis)
    parts = [x] + [_ring(x, axis, n, k) for k in range(1, n)]
    stack = jnp.stack(parts[::-1] + parts[:0:-1])
    out = lax.dynamic_slice_in_dim(stack, n - 1 - c, n, axis=0)
    return out.reshape((n * x.shape[0],) + x.shape[1:])


def gather_ring4(x, axis):
    h = x.shape[0] // 2
    p1 = _ring(x, axis, 4, 1)
    m1 = _ring(x, axis, 4, -1)
    f = _ring(p1[:h], axis, 4, 1)
    g = _ring(m1[h:], axis, 4, -1)
    return [x, m1, jnp.concatenate([f, g]), p1]


def scatter_ring4(blocks, axis):
    b0, b1, b2, b3 = blocks
    h = b0.shape[0] // 2
    bf = jnp.bfloat16
    got_p = _ring(jnp.concatenate([b1[h:], b2[:h]]).astype(bf), axis, 4, 1)
    got_m = _ring(jnp.concatenate([b3[:h], b2[h:]]).astype(bf), axis, 4, -1)
    s1p, x1 = got_p[:h], got_p[h:]
    s1m, y1 = got_m[:h], got_m[h:]
    s2p = _ring((b1[:h] + x1.astype(jnp.float32)).astype(bf), axis, 4, 1)
    s2m = _ring((b3[h:] + y1.astype(jnp.float32)).astype(bf), axis, 4, -1)
    f32 = jnp.float32
    top = b0[:h] + s2p.astype(f32) + s1m.astype(f32)
    bot = b0[h:] + s1p.astype(f32) + s2m.astype(f32)
    return jnp.concatenate([top, bot])


def scatter_line(x, axis, n):
    c = lax.axis_index(axis)
    rows = x.shape[0] // n
    acc = lax.dynamic_slice_in_dim(x, c * rows, rows, axis=0)
    for k in range(1, n):
        part = lax.dynamic_slice_in_dim(x, ((c + k) % n) * rows, rows, axis=0)
        acc = acc + _ring(part.astype(jnp.bfloat16), axis, n, k).astype(jnp.float32)
    return acc


def local(cotangent, gate_pre, up_pre, w_down):
    gate_wide = gate_pre.astype(jnp.float32)
    up_wide = up_pre.astype(jnp.float32)
    sigmoid_gate = jax.nn.sigmoid(gate_wide)
    activated = gate_wide * sigmoid_gate
    hidden = (activated * up_wide).astype(jnp.bfloat16)
    ndp = lax.axis_size("dp")
    nctx = lax.axis_size("ctx")
    groups = ndp * nctx
    a = lax.axis_index("dp")

    span_rs = w_down.shape[0] * nctx
    partial = lax.dot_general(
        cotangent, hidden, (((0,), (0,)), ((), ())), preferred_element_type=jnp.float32
    )
    blocks = [lax.dynamic_slice_in_dim(partial, ((a + k) % ndp) * span_rs, span_rs, axis=0) for k in range(4)]
    w_down, blocks = lax.optimization_barrier((w_down, blocks))
    reduced = scatter_ring4(blocks, "dp")
    summed = scatter_line(reduced, "ctx", nctx)
    w_ctx = gather_line(w_down, "ctx", nctx)
    span = w_ctx.shape[0]
    grad_hidden = None
    for k, blk in enumerate(gather_ring4(w_ctx, "dp")):
        cols = lax.dynamic_slice_in_dim(cotangent, ((a + k) % ndp) * span, span, axis=1)
        term = jnp.dot(cols, blk, preferred_element_type=jnp.float32)
        grad_hidden = term if grad_hidden is None else grad_hidden + term
    grad_gate = (
        grad_hidden * up_wide * sigmoid_gate * (1.0 + gate_wide * (1.0 - sigmoid_gate))
    ).astype(jnp.bfloat16)
    grad_up = (grad_hidden * activated).astype(jnp.bfloat16)

    grad_down = (summed / groups).astype(jnp.bfloat16)
    return (grad_gate, grad_up, grad_down)


def solution(mesh):
    in_specs = (
        P(("dp", "ctx"), None),
        P(("dp", "ctx"), "tp"),
        P(("dp", "ctx"), "tp"),
        P(("dp", "ctx"), "tp"),
    )
    out_specs = (P(("dp", "ctx"), "tp"), P(("dp", "ctx"), "tp"), P(("dp", "ctx"), "tp"))
    return jax.shard_map(local, mesh=mesh, in_specs=in_specs, out_specs=out_specs, check_vma=False)
```

```python
import jax
import jax.numpy as jnp
from jax import lax
from jax.sharding import PartitionSpec as P


def _line(x, axis, n, k):
    return lax.ppermute(x, axis, [(i, i + k) for i in range(n) if 0 <= i + k < n])


def _ring(x, axis, n, k):
    return lax.ppermute(x, axis, [(i, (i + k) % n) for i in range(n)])


def gather_line(x, axis, n):
    c = lax.axis_index(axis)
    parts = [x] + [_ring(x, axis, n, k) for k in range(1, n)]
    return jnp.concatenate([lax.select_n((c - s) % n, *parts) for s in range(n)])


def gather_ring4(x, axis):
    h = x.shape[0] // 2
    p1 = _ring(x, axis, 4, 1)
    m1 = _ring(x, axis, 4, -1)
    f = _ring(p1[:h], axis, 4, 1)
    g = _ring(m1[h:], axis, 4, -1)
    return [x, m1, jnp.concatenate([f, g]), p1]


def scatter_ring4(blocks, axis):
    b0, b1, b2, b3 = blocks
    h = b0.shape[0] // 2
    bf = jnp.bfloat16
    got_p = _ring(jnp.concatenate([b1[h:], b2[:h]]).astype(bf), axis, 4, 1)
    got_m = _ring(jnp.concatenate([b3[:h], b2[h:]]).astype(bf), axis, 4, -1)
    s1p, x1 = got_p[:h], got_p[h:]
    s1m, y1 = got_m[:h], got_m[h:]
    s2p = _ring((b1[:h] + x1.astype(jnp.float32)).astype(bf), axis, 4, 1)
    s2m = _ring((b3[h:] + y1.astype(jnp.float32)).astype(bf), axis, 4, -1)
    f32 = jnp.float32
    top = b0[:h] + s2p.astype(f32) + s1m.astype(f32)
    bot = b0[h:] + s1p.astype(f32) + s2m.astype(f32)
    return jnp.concatenate([top, bot])


def scatter_line(x, axis, n):
    c = lax.axis_index(axis)
    rows = x.shape[0] // n
    acc = lax.dynamic_slice_in_dim(x, c * rows, rows, axis=0)
    for k in range(1, n):
        part = lax.dynamic_slice_in_dim(x, ((c + k) % n) * rows, rows, axis=0)
        acc = acc + _ring(part.astype(jnp.bfloat16), axis, n, k).astype(jnp.float32)
    return acc


def local(cotangent, gate_pre, up_pre, w_down):
    gate_wide = gate_pre.astype(jnp.float32)
    up_wide = up_pre.astype(jnp.float32)
    sigmoid_gate = jax.nn.sigmoid(gate_wide)
    activated = gate_wide * sigmoid_gate
    hidden = (activated * up_wide).astype(jnp.bfloat16)
    ndp = lax.axis_size("dp")
    nctx = lax.axis_size("ctx")
    groups = ndp * nctx
    a = lax.axis_index("dp")

    span_rs = w_down.shape[0] * nctx
    partial = lax.dot_general(
        cotangent, hidden, (((0,), (0,)), ((), ())), preferred_element_type=jnp.float32
    )
    blocks = [lax.dynamic_slice_in_dim(partial, ((a + k) % ndp) * span_rs, span_rs, axis=0) for k in range(4)]
    w_down, blocks = lax.optimization_barrier((w_down, blocks))
    reduced = scatter_ring4(blocks, "dp")
    summed = scatter_line(reduced, "ctx", nctx)
    w_ctx = gather_line(w_down, "ctx", nctx)
    span = w_ctx.shape[0]
    grad_hidden = None
    for k, blk in enumerate(gather_ring4(w_ctx, "dp")):
        cols = lax.dynamic_slice_in_dim(cotangent, ((a + k) % ndp) * span, span, axis=1)
        term = jnp.dot(cols, blk, preferred_element_type=jnp.float32)
        grad_hidden = term if grad_hidden is None else grad_hidden + term
    grad_gate = (
        grad_hidden * up_wide * sigmoid_gate * (1.0 + gate_wide * (1.0 - sigmoid_gate))
    ).astype(jnp.bfloat16)
    grad_up = (grad_hidden * activated).astype(jnp.bfloat16)

    grad_down = (summed / groups).astype(jnp.bfloat16)
    return (grad_gate, grad_up, grad_down)


def solution(mesh):
    in_specs = (
        P(("dp", "ctx"), None),
        P(("dp", "ctx"), "tp"),
        P(("dp", "ctx"), "tp"),
        P(("dp", "ctx"), "tp"),
    )
    out_specs = (P(("dp", "ctx"), "tp"), P(("dp", "ctx"), "tp"), P(("dp", "ctx"), "tp"))
    return jax.shard_map(local, mesh=mesh, in_specs=in_specs, out_specs=out_specs, check_vma=False)
```

```python
import jax
import jax.numpy as jnp
from jax import lax
from jax.sharding import PartitionSpec as P


def _line(x, axis, n, k):
    return lax.ppermute(x, axis, [(i, i + k) for i in range(n) if 0 <= i + k < n])


def _ring(x, axis, n, k):
    return lax.ppermute(x, axis, [(i, (i + k) % n) for i in range(n)])


def gather_line(x, axis, n):
    c = lax.axis_index(axis)
    parts = [x] + [_ring(x, axis, n, k) for k in range(1, n)]
    return jnp.concatenate([lax.select_n((c - s) % n, *parts) for s in range(n)])


def gather_ring4(x, axis):
    h = x.shape[0] // 2
    p1 = _ring(x, axis, 4, 1)
    m1 = _ring(x, axis, 4, -1)
    f = _ring(p1[:h], axis, 4, 1)
    g = _ring(m1[h:], axis, 4, -1)
    return [x, m1, jnp.concatenate([f, g]), p1]


def scatter_ring4(blocks, axis):
    b0, b1, b2, b3 = blocks
    h = b0.shape[0] // 2
    bf = jnp.bfloat16
    got_p = _ring(jnp.concatenate([b1[h:], b2[:h]]).astype(bf), axis, 4, 1)
    got_m = _ring(jnp.concatenate([b3[:h], b2[h:]]).astype(bf), axis, 4, -1)
    s1p, x1 = got_p[:h], got_p[h:]
    s1m, y1 = got_m[:h], got_m[h:]
    s2p = _ring((b1[:h] + x1.astype(jnp.float32)).astype(bf), axis, 4, 1)
    s2m = _ring((b3[h:] + y1.astype(jnp.float32)).astype(bf), axis, 4, -1)
    f32 = jnp.float32
    top = b0[:h] + s2p.astype(f32) + s1m.astype(f32)
    bot = b0[h:] + s1p.astype(f32) + s2m.astype(f32)
    return jnp.concatenate([top, bot])


def scatter_line(x, axis, n):
    c = lax.axis_index(axis)
    rows = x.shape[0] // n
    acc = lax.dynamic_slice_in_dim(x, c * rows, rows, axis=0)
    for k in range(1, n):
        part = lax.dynamic_slice_in_dim(x, ((c + k) % n) * rows, rows, axis=0)
        acc = acc + _ring(part.astype(jnp.bfloat16), axis, n, k).astype(jnp.float32)
    return acc


def local(cotangent, gate_pre, up_pre, w_down):
    gate_wide = gate_pre.astype(jnp.float32)
    up_wide = up_pre.astype(jnp.float32)
    sigmoid_gate = jax.nn.sigmoid(gate_wide)
    activated = gate_wide * sigmoid_gate
    hidden = (activated * up_wide).astype(jnp.bfloat16)
    ndp = lax.axis_size("dp")
    nctx = lax.axis_size("ctx")
    groups = ndp * nctx
    a = lax.axis_index("dp")

    span_rs = w_down.shape[0] * nctx
    partial = lax.dot_general(
        cotangent, hidden, (((0,), (0,)), ((), ())), preferred_element_type=jnp.float32
    )
    blocks = [lax.dynamic_slice_in_dim(partial, ((a + k) % ndp) * span_rs, span_rs, axis=0) for k in range(4)]
    w_down, blocks = lax.optimization_barrier((w_down, blocks))
    reduced = scatter_ring4(blocks, "dp")
    got = lax.all_to_all(reduced.astype(jnp.bfloat16), "ctx", 0, 0, tiled=True)
    summed = got.astype(jnp.float32).reshape((nctx, -1) + got.shape[1:]).sum(axis=0)
    w_ctx = gather_line(w_down, "ctx", nctx)
    span = w_ctx.shape[0]
    grad_hidden = None
    for k, blk in enumerate(gather_ring4(w_ctx, "dp")):
        cols = lax.dynamic_slice_in_dim(cotangent, ((a + k) % ndp) * span, span, axis=1)
        term = jnp.dot(cols, blk, preferred_element_type=jnp.float32)
        grad_hidden = term if grad_hidden is None else grad_hidden + term
    grad_gate = (
        grad_hidden * up_wide * sigmoid_gate * (1.0 + gate_wide * (1.0 - sigmoid_gate))
    ).astype(jnp.bfloat16)
    grad_up = (grad_hidden * activated).astype(jnp.bfloat16)

    grad_down = (summed / groups).astype(jnp.bfloat16)
    return (grad_gate, grad_up, grad_down)


def solution(mesh):
    in_specs = (
        P(("dp", "ctx"), None),
        P(("dp", "ctx"), "tp"),
        P(("dp", "ctx"), "tp"),
        P(("dp", "ctx"), "tp"),
    )
    out_specs = (P(("dp", "ctx"), "tp"), P(("dp", "ctx"), "tp"), P(("dp", "ctx"), "tp"))
    return jax.shard_map(local, mesh=mesh, in_specs=in_specs, out_specs=out_specs, check_vma=False)
```
